512 devices in a mesh: col: 64 (over z_lo, y, core), row: 8 (over x, z_hi).
Axes of the slice: x: 4, y: 8, z: 8 (z_hi: 2, z_lo: 4; z = z_hi * 4 + z_lo), core: 2. Of those that a mesh axis runs over, the one named last changes fastest.
Arguments:
- image: bfloat16 [96, 64, 8192], P(None, 'row', 'col'), may hold values from -6 to 6
- cotangent: bfloat16 [96, 64, 8192], P(None, 'row', 'col'), may hold values from -6 to 6
- dw_kernel: float32 [96, 7, 7], replicated, may hold values from -0.875 to 0.875
- dw_bias: float32 [96], replicated, may hold values from -3 to 3
- ln_gain: float32 [96], replicated, may hold values from 0.1 to 1.9
- ln_bias: float32 [96], replicated, may hold values from -3 to 3
- w_in: bfloat16 [96, 384], replicated, may hold values from -0.625 to 0.625
- b_in: float32 [384], replicated, may hold values from -3 to 3
- w_out: bfloat16 [384, 96], replicated, may hold values from -0.3125 to 0.3125
- layer_scale: float32 [96], replicated, may hold values from 0.5 to 2
Outputs:
- block_out: bfloat16 [96, 64, 8192], P(None, 'row', 'col')
- image_grad: bfloat16 [96, 64, 8192], P(None, 'row', 'col')
- kernel_grad: float32 [96, 7, 7], replicated
- dw_bias_grad: float32 [96], replicated
- gain_grad: float32 [96], replicated
- ln_bias_grad: float32 [96], replicated
- w_in_grad: float32 [96, 384], replicated
- b_in_grad: float32 [384], replicated
- w_out_grad: float32 [384, 96], replicated
- scale_grad: float32 [96], replicated
The draws below stay inside these ranges and needn't reach their ends.
All inputs are finite; a program needn't handle non-finite values.
Results may differ from the reference program's by a relative error of at most 0.0065.
Values may be sent and summed in bfloat16 or wider, within the bound.
No kernel may reach another device: no remote copies, remote signals or barrier semaphores. Data moves between devices by JAX's collectives and lax.ppermute only.
A program may use at most 64 MiB of HBM per device.

```python
import math
import jax
import jax.numpy as jnp
from jax import lax

C = 96
HID = 384
H = 64
W = 8192


def steps_of(own_key, extent, cuts, smallest, top_value):
    factor_of = 1.0
    for axis_at, blocks in cuts:
        draws = jax.random.uniform(jax.random.fold_in(jax.random.fold_in(own_key, 6), axis_at), (blocks,), jnp.float32, smallest / len(cuts), top_value / len(cuts))
        factor_of = factor_of * jnp.repeat(jnp.exp(draws), extent[axis_at] // blocks).reshape((-1,) + (1,) * (len(extent) - 1 - axis_at))
    return factor_of


def gaussian(rng, extent, scale, most, shards=(), dtype=jnp.bfloat16):
    result = jax.random.normal(rng, extent, jnp.float32) * scale
    if len(shards) > 0:
        result = steps_of(rng, extent, shards, -0.22, 0.18) * result
    return jnp.clip(result, min=-most, max=most).astype(dtype)


def setup_inputs(seed: int = 0) -> dict:
    seeds = jax.random.split(jax.random.key(seed), 11)
    return {
        "image": gaussian(seeds[0], (C, H, W), 1.0, 6.0, ((1, 8), (2, 64))),
        "cotangent": gaussian(seeds[1], (C, H, W), 1.0, 6.0, ((1, 8), (2, 64))),
        "dw_kernel": gaussian(seeds[2], (C, 7, 7), 49 ** -0.5, 0.875, (), jnp.float32),
        "dw_bias": gaussian(seeds[3], (C,), 0.5, 3.0, (), jnp.float32),
        "ln_gain": jnp.clip(1.0 + 0.18 * jax.random.normal(seeds[4], (C,), jnp.float32), 0.1, 1.9),
        "ln_bias": gaussian(seeds[5], (C,), 0.5, 3.0, (), jnp.float32),
        "w_in": gaussian(seeds[6], (C, HID), C ** -0.5, 0.625),
        "b_in": gaussian(seeds[7], (HID,), 0.5, 3.0, (), jnp.float32),
        "w_out": gaussian(seeds[8], (HID, C), HID ** -0.5, 0.3125),
        "layer_scale": jnp.clip(jnp.exp(jax.random.uniform(seeds[9], (C,), jnp.float32, math.log(0.5), math.log(2.0))), 0.5, 2.0),
    }


def conv_seven(padded, kernel):
    height = padded.shape[1] - 6
    breadth = padded.shape[2] - 6
    summed = jnp.zeros((padded.shape[0], height, breadth), jnp.float32)
    for row_step in range(7):
        for col_step in range(7):
            summed = summed + kernel[:, row_step, col_step][:, None, None] * padded[:, row_step:row_step + height, col_step:col_step + breadth]
    return summed

def kernel_terms(conv_grad, padded):
    height, breadth = (conv_grad.shape[1], conv_grad.shape[2])
    pieces = []
    for row_step in range(7):
        for col_step in range(7):
            pieces.append(lax.optimization_barrier(jnp.sum(conv_grad * padded[:, row_step:row_step + height, col_step:col_step + breadth], axis=(1, 2))))
    return jnp.stack(pieces, axis=1).reshape(conv_grad.shape[0], 7, 7)

def product(form, left, right):
    return jnp.einsum(form, left.astype(jnp.float32), right.astype(jnp.float32), precision=lax.Precision.HIGHEST)

def mixing(conv_flat, image_flat, cotan_flat, ln_gain, ln_bias, w_in, b_in, w_out, layer_scale):
    average = lax.optimization_barrier(jnp.mean(conv_flat, axis=0, keepdims=True))
    centred = conv_flat - average
    spread = lax.optimization_barrier(jnp.mean(centred * centred, axis=0, keepdims=True))
    inverse = lax.rsqrt(spread + 1e-06)
    normed = centred * inverse
    ln_out = (normed * ln_gain[:, None] + ln_bias[:, None]).astype(jnp.bfloat16)
    pre_act = product('ch,cp->hp', w_in, ln_out) + b_in[:, None]
    act_out, gelu_pull = jax.vjp(jax.nn.gelu, pre_act)
    activ = act_out.astype(jnp.bfloat16)
    branch = product('hc,hp->cp', w_out, activ)
    scale_col = layer_scale[:, None]
    block_out = (image_flat.astype(jnp.float32) + scale_col * branch).astype(jnp.bfloat16)
    upstream = cotan_flat.astype(jnp.float32)
    scale_sum = lax.optimization_barrier(jnp.sum(upstream * branch, axis=1))
    branch_grad = (scale_col * upstream).astype(jnp.bfloat16)
    w_out_sum = product('hp,cp->hc', activ, branch_grad)
    act_grad = product('hc,cp->hp', w_out, branch_grad)
    pre_grad = gelu_pull(act_grad)[0].astype(jnp.bfloat16)
    b_in_sum = lax.optimization_barrier(jnp.sum(pre_grad.astype(jnp.float32), axis=1))
    w_in_sum = product('cp,hp->ch', ln_out, pre_grad)
    ln_grad = product('ch,hp->cp', w_in, pre_grad)
    gain_sum = lax.optimization_barrier(jnp.sum(ln_grad * normed, axis=1))
    shift_sum = lax.optimization_barrier(jnp.sum(ln_grad, axis=1))
    normed_grad = ln_grad * ln_gain[:, None]
    conv_grad = inverse * (normed_grad - lax.optimization_barrier(jnp.mean(normed_grad, axis=0, keepdims=True)) - normed * lax.optimization_barrier(jnp.mean(normed_grad * normed, axis=0, keepdims=True)))
    return (block_out, conv_grad, (gain_sum, shift_sum, w_in_sum, b_in_sum, w_out_sum, scale_sum))

def reference(image, cotangent, dw_kernel, dw_bias, ln_gain, ln_bias, w_in, b_in, w_out, layer_scale):
    padded = jnp.pad(image.astype(jnp.float32), ((0, 0), (3, 3), (3, 3)))
    conv_out = conv_seven(padded, dw_kernel) + dw_bias[:, None, None]
    block_rows = 16
    blocks = H // block_rows

    def split_blocks(field):
        return field.reshape(C, blocks, block_rows * W).transpose(1, 0, 2)

    def join_blocks(field):
        return field.transpose(1, 0, 2).reshape(C, H, W)
    start = (jnp.zeros((C,), jnp.float32), jnp.zeros((C,), jnp.float32), jnp.zeros((C, HID), jnp.float32), jnp.zeros((HID,), jnp.float32), jnp.zeros((HID, C), jnp.float32), jnp.zeros((C,), jnp.float32))

    def advance(carried, element):
        conv_part, image_part, cotan_part = element
        out_part, grad_part, sums = mixing(conv_part, image_part, cotan_part, ln_gain, ln_bias, w_in, b_in, w_out, layer_scale)
        return (tuple((old + new for old, new in zip(carried, sums))), (out_part, grad_part))
    totals, (out_blocks, grad_blocks) = lax.scan(advance, start, (split_blocks(conv_out), split_blocks(image), split_blocks(cotangent)))
    block_out = join_blocks(out_blocks)
    conv_grad = join_blocks(grad_blocks)
    flipped = dw_kernel[:, ::-1, ::-1]
    back = conv_seven(jnp.pad(conv_grad, ((0, 0), (3, 3), (3, 3))), flipped)
    image_grad = (cotangent.astype(jnp.float32) + back).astype(jnp.bfloat16)
    kernel_sum = kernel_terms(conv_grad, padded)
    bias_sum = lax.optimization_barrier(jnp.sum(conv_grad, axis=(1, 2)))
    factor = 1.0 / math.sqrt(H * W)
    gain_sum, shift_sum, w_in_sum, b_in_sum, w_out_sum, scale_sum = totals
    return (block_out, image_grad, factor * kernel_sum, factor * bias_sum, factor * gain_sum, factor * shift_sum, factor * w_in_sum, factor * b_in_sum, factor * w_out_sum, factor * scale_sum)
```

```python
import math

import jax
import jax.numpy as jnp
from jax import lax
from jax.sharding import PartitionSpec as P


def padded_2(block, sides, width):
    for axis, dim in sides:
        count = lax.axis_size(axis)
        forward = [(i, i + 1) for i in range(count - 1)]
        backward = [(target, source) for source, target in forward]
        low = lax.ppermute(
            lax.slice_in_dim(block, block.shape[dim] - width, None, axis=dim), axis, forward
        )
        high = lax.ppermute(lax.slice_in_dim(block, 0, width, axis=dim), axis, backward)
        block = jnp.concatenate([low, block, high], axis=dim)
    return block


def from_behind(value, axis, steps):
    count = lax.axis_size(axis)
    initial, last = (max(0, -steps), min(count, count - steps))
    return lax.ppermute(value, axis, [(source, source + steps) for source in range(initial, last)])


def conv_seven(padded, kernel):
    height = padded.shape[1] - 6
    breadth = padded.shape[2] - 6
    summed = jnp.zeros((padded.shape[0], height, breadth), jnp.float32)
    for row_step in range(7):
        for col_step in range(7):
            summed = (
                summed
                + kernel[:, row_step, col_step][:, None, None]
                * padded[:, row_step : row_step + height, col_step : col_step + breadth]
            )
    return summed


def kernel_terms(conv_grad, padded):
    height, breadth = (conv_grad.shape[1], conv_grad.shape[2])
    pieces = []
    for row_step in range(7):
        for col_step in range(7):
            pieces.append(
                jnp.sum(
                    conv_grad
                    * padded[:, row_step : row_step + height, col_step : col_step + breadth],
                    axis=(1, 2),
                )
            )
    return jnp.stack(pieces, axis=1).reshape(conv_grad.shape[0], 7, 7)


def butterfly_sum(parts):
    shapes = [p.shape for p in parts]
    flat = jnp.concatenate([p.reshape(-1) for p in parts])
    for axis in ("col", "row"):
        count = lax.axis_size(axis)
        bit = 1
        while bit < count:
            pairs = [(i, i ^ bit) for i in range(count)]
            flat = flat + lax.ppermute(flat, axis, pairs)
            bit *= 2
    out, start = [], 0
    for shape in shapes:
        size = math.prod(shape)
        out.append(flat[start : start + size].reshape(shape))
        start += size
    return tuple(out)


def product(form, left, right):
    return jnp.einsum(form, left, right, preferred_element_type=jnp.float32)


def mixing(conv_flat, image_flat, cotan_flat, ln_gain, ln_bias, w_in, b_in, w_out, layer_scale):
    average = jnp.mean(conv_flat, axis=0, keepdims=True)
    centred = conv_flat - average
    spread = jnp.mean(centred * centred, axis=0, keepdims=True)
    inverse = lax.rsqrt(spread + 1e-06)
    normed = centred * inverse
    ln_out = (normed * ln_gain[:, None] + ln_bias[:, None]).astype(jnp.bfloat16)
    pre_act = product("ch,cp->hp", w_in, ln_out) + b_in[:, None]
    act_out, gelu_pull = jax.vjp(jax.nn.gelu, pre_act)
    activ = act_out.astype(jnp.bfloat16)
    branch = product("hc,hp->cp", w_out, activ)
    scale_col = layer_scale[:, None]
    block_out = (image_flat.astype(jnp.float32) + scale_col * branch).astype(jnp.bfloat16)
    upstream = cotan_flat.astype(jnp.float32)
    scale_sum = jnp.sum(upstream * branch, axis=1)
    branch_grad = (scale_col * upstream).astype(jnp.bfloat16)
    w_out_sum = product("hp,cp->hc", activ, branch_grad)
    act_grad = product("hc,cp->hp", w_out, branch_grad)
    pre_grad = gelu_pull(act_grad)[0].astype(jnp.bfloat16)
    b_in_sum = jnp.sum(pre_grad.astype(jnp.float32), axis=1)
    w_in_sum = product("cp,hp->ch", ln_out, pre_grad)
    ln_grad = product("ch,hp->cp", w_in, pre_grad)
    gain_sum = jnp.sum(ln_grad * normed, axis=1)
    shift_sum = jnp.sum(ln_grad, axis=1)
    normed_grad = ln_grad * ln_gain[:, None]
    conv_grad = inverse * (
        normed_grad
        - jnp.mean(normed_grad, axis=0, keepdims=True)
        - normed * jnp.mean(normed_grad * normed, axis=0, keepdims=True)
    )
    return (block_out, conv_grad, (gain_sum, shift_sum, w_in_sum, b_in_sum, w_out_sum, scale_sum))


def local(image, cotangent, dw_kernel, dw_bias, ln_gain, ln_bias, w_in, b_in, w_out, layer_scale):
    channels, height, breadth = image.shape
    pixels = height * breadth
    padded = padded_2(image, (("col", 2), ("row", 1)), 3)
    conv_out = conv_seven(padded, dw_kernel) + dw_bias[:, None, None]
    block_flat, grad_flat, sums = mixing(
        conv_out.reshape(channels, pixels),
        image.reshape(channels, pixels),
        cotangent.reshape(channels, pixels),
        ln_gain,
        ln_bias,
        w_in,
        b_in,
        w_out,
        layer_scale,
    )
    gain_sum, shift_sum, w_in_sum, b_in_sum, w_out_sum, scale_sum = sums
    block_out = block_flat.reshape(channels, height, breadth)
    conv_grad = grad_flat.reshape(channels, height, breadth)
    flipped = dw_kernel[:, ::-1, ::-1]
    extended = conv_seven(jnp.pad(conv_grad, ((0, 0), (6, 6), (6, 6))), flipped)
    from_above = from_behind(extended[:, height + 3 :, :].astype(jnp.bfloat16), "row", 1).astype(
        jnp.float32
    )
    from_below = from_behind(extended[:, :3, :].astype(jnp.bfloat16), "row", -1).astype(jnp.float32)
    middle = extended[:, 3 : height + 3, :]
    middle = (
        middle
        + jnp.pad(from_above, ((0, 0), (0, height - 3), (0, 0)))
        + jnp.pad(from_below, ((0, 0), (height - 3, 0), (0, 0)))
    )
    from_left = from_behind(middle[:, :, breadth + 3 :], "col", 1)
    from_right = from_behind(middle[:, :, :3], "col", -1)
    back = middle[:, :, 3 : breadth + 3]
    back = (
        back
        + jnp.pad(from_left, ((0, 0), (0, 0), (0, breadth - 3)))
        + jnp.pad(from_right, ((0, 0), (0, 0), (breadth - 3, 0)))
    )
    image_grad = (cotangent.astype(jnp.float32) + back).astype(jnp.bfloat16)
    kernel_sum = kernel_terms(conv_grad, padded)
    bias_sum = jnp.sum(conv_grad, axis=(1, 2))
    kernel_sum, bias_sum, gain_sum, shift_sum, w_in_sum, b_in_sum, w_out_sum, scale_sum = butterfly_sum(
        (kernel_sum, bias_sum, gain_sum, shift_sum, w_in_sum, b_in_sum, w_out_sum, scale_sum)
    )
    factor = 1.0 / math.sqrt(height * lax.axis_size("row") * breadth * lax.axis_size("col"))
    return (
        block_out,
        image_grad,
        factor * kernel_sum,
        factor * bias_sum,
        factor * gain_sum,
        factor * shift_sum,
        factor * w_in_sum,
        factor * b_in_sum,
        factor * w_out_sum,
        factor * scale_sum,
    )


def solution(mesh):
    in_specs = (
        P(None, "row", "col"),
        P(None, "row", "col"),
        P(),
        P(),
        P(),
        P(),
        P(),
        P(),
        P(),
        P(),
    )
    out_specs = (
        P(None, "row", "col"),
        P(None, "row", "col"),
        P(),
        P(),
        P(),
        P(),
        P(),
        P(),
        P(),
        P(),
    )
    return jax.shard_map(local, mesh=mesh, in_specs=in_specs, out_specs=out_specs, check_vma=False)
```

```python
import math

import jax
import jax.numpy as jnp
from jax import lax
from jax.sharding import PartitionSpec as P


def padded_2(block, sides, width):
    for axis, dim in sides:
        count = lax.axis_size(axis)
        forward = [(i, i + 1) for i in range(count - 1)]
        backward = [(target, source) for source, target in forward]
        low = lax.ppermute(
            lax.slice_in_dim(block, block.shape[dim] - width, None, axis=dim), axis, forward
        )
        high = lax.ppermute(lax.slice_in_dim(block, 0, width, axis=dim), axis, backward)
        block = jnp.concatenate([low, block, high], axis=dim)
    return block


def from_behind(value, axis, steps):
    count = lax.axis_size(axis)
    initial, last = (max(0, -steps), min(count, count - steps))
    return lax.ppermute(value, axis, [(source, source + steps) for source in range(initial, last)])


def conv_seven(padded, kernel):
    height = padded.shape[1] - 6
    breadth = padded.shape[2] - 6
    summed = jnp.zeros((padded.shape[0], height, breadth), jnp.float32)
    for row_step in range(7):
        for col_step in range(7):
            summed = (
                summed
                + kernel[:, row_step, col_step][:, None, None]
                * padded[:, row_step : row_step + height, col_step : col_step + breadth]
            )
    return summed


def kernel_terms(conv_grad, padded):
    height, breadth = (conv_grad.shape[1], conv_grad.shape[2])
    pieces = []
    for row_step in range(7):
        for col_step in range(7):
            pieces.append(
                jnp.sum(
                    conv_grad
                    * padded[:, row_step : row_step + height, col_step : col_step + breadth],
                    axis=(1, 2),
                )
            )
    return jnp.stack(pieces, axis=1).reshape(conv_grad.shape[0], 7, 7)


def xor_partner(value, axis, mask):
    return lax.ppermute(value, axis, [(i, i ^ mask) for i in range(lax.axis_size(axis))])


def butterfly_sum(parts, halving=(("col", 1), ("col", 2))):
    shapes = [p.shape for p in parts]
    flat = jnp.concatenate([p.reshape(-1) for p in parts])
    total = flat.shape[0]
    unit = 2 ** len(halving)
    flat = jnp.pad(flat, (0, -total % unit))
    doubling = []
    for axis in ("col", "row"):
        mask = 1
        while mask < lax.axis_size(axis):
            if (axis, mask) not in halving:
                doubling.append((axis, mask))
            mask *= 2
    sides = []
    for axis, mask in halving:
        half = flat.shape[0] // 2
        side = (lax.axis_index(axis) // mask) % 2
        keep = lax.dynamic_slice_in_dim(flat, side * half, half)
        send = lax.dynamic_slice_in_dim(flat, (1 - side) * half, half)
        flat = keep + xor_partner(send, axis, mask)
        sides.append(side)
    for axis, mask in doubling:
        flat = flat + xor_partner(flat, axis, mask)
    for (axis, mask), side in zip(reversed(halving), reversed(sides)):
        other = xor_partner(flat, axis, mask)
        flat = jnp.where(side == 0, jnp.concatenate([flat, other]), jnp.concatenate([other, flat]))
    out, start = [], 0
    for shape in shapes:
        size = math.prod(shape)
        out.append(flat[start : start + size].reshape(shape))
        start += size
    return tuple(out)


def product(form, left, right):
    return jnp.einsum(form, left, right, preferred_element_type=jnp.float32)


def mixing(conv_flat, image_flat, cotan_flat, ln_gain, ln_bias, w_in, b_in, w_out, layer_scale):
    average = jnp.mean(conv_flat, axis=0, keepdims=True)
    centred = conv_flat - average
    spread = jnp.mean(centred * centred, axis=0, keepdims=True)
    inverse = lax.rsqrt(spread + 1e-06)
    normed = centred * inverse
    ln_out = (normed * ln_gain[:, None] + ln_bias[:, None]).astype(jnp.bfloat16)
    pre_act = product("ch,cp->hp", w_in, ln_out) + b_in[:, None]
    act_out, gelu_pull = jax.vjp(jax.nn.gelu, pre_act)
    activ = act_out.astype(jnp.bfloat16)
    branch = product("hc,hp->cp", w_out, activ)
    scale_col = layer_scale[:, None]
    block_out = (image_flat.astype(jnp.float32) + scale_col * branch).astype(jnp.bfloat16)
    upstream = cotan_flat.astype(jnp.float32)
    scale_sum = jnp.sum(upstream * branch, axis=1)
    branch_grad = (scale_col * upstream).astype(jnp.bfloat16)
    w_out_sum = product("hp,cp->hc", activ, branch_grad)
    act_grad = product("hc,cp->hp", w_out, branch_grad)
    pre_grad = gelu_pull(act_grad)[0].astype(jnp.bfloat16)
    b_in_sum = jnp.sum(pre_grad.astype(jnp.float32), axis=1)
    w_in_sum = product("cp,hp->ch", ln_out, pre_grad)
    ln_grad = product("ch,hp->cp", w_in, pre_grad)
    gain_sum = jnp.sum(ln_grad * normed, axis=1)
    shift_sum = jnp.sum(ln_grad, axis=1)
    normed_grad = ln_grad * ln_gain[:, None]
    conv_grad = inverse * (
        normed_grad
        - jnp.mean(normed_grad, axis=0, keepdims=True)
        - normed * jnp.mean(normed_grad * normed, axis=0, keepdims=True)
    )
    return (block_out, conv_grad, (gain_sum, shift_sum, w_in_sum, b_in_sum, w_out_sum, scale_sum))


def local(image, cotangent, dw_kernel, dw_bias, ln_gain, ln_bias, w_in, b_in, w_out, layer_scale):
    channels, height, breadth = image.shape
    pixels = height * breadth
    padded = padded_2(image, (("col", 2), ("row", 1)), 3)
    conv_out = conv_seven(padded, dw_kernel) + dw_bias[:, None, None]
    block_flat, grad_flat, sums = mixing(
        conv_out.reshape(channels, pixels),
        image.reshape(channels, pixels),
        cotangent.reshape(channels, pixels),
        ln_gain,
        ln_bias,
        w_in,
        b_in,
        w_out,
        layer_scale,
    )
    gain_sum, shift_sum, w_in_sum, b_in_sum, w_out_sum, scale_sum = sums
    block_out = block_flat.reshape(channels, height, breadth)
    conv_grad = grad_flat.reshape(channels, height, breadth)
    flipped = dw_kernel[:, ::-1, ::-1]
    extended = conv_seven(jnp.pad(conv_grad, ((0, 0), (6, 6), (6, 6))), flipped)
    from_above = from_behind(extended[:, height + 3 :, :].astype(jnp.bfloat16), "row", 1).astype(
        jnp.float32
    )
    from_below = from_behind(extended[:, :3, :].astype(jnp.bfloat16), "row", -1).astype(jnp.float32)
    middle = extended[:, 3 : height + 3, :]
    middle = (
        middle
        + jnp.pad(from_above, ((0, 0), (0, height - 3), (0, 0)))
        + jnp.pad(from_below, ((0, 0), (height - 3, 0), (0, 0)))
    )
    from_left = from_behind(middle[:, :, breadth + 3 :], "col", 1)
    from_right = from_behind(middle[:, :, :3], "col", -1)
    back = middle[:, :, 3 : breadth + 3]
    back = (
        back
        + jnp.pad(from_left, ((0, 0), (0, 0), (0, breadth - 3)))
        + jnp.pad(from_right, ((0, 0), (0, 0), (breadth - 3, 0)))
    )
    image_grad = (cotangent.astype(jnp.float32) + back).astype(jnp.bfloat16)
    kernel_sum = kernel_terms(conv_grad, padded)
    bias_sum = jnp.sum(conv_grad, axis=(1, 2))
    kernel_sum, bias_sum, gain_sum, shift_sum, w_in_sum, b_in_sum, w_out_sum, scale_sum = butterfly_sum(
        (kernel_sum, bias_sum, gain_sum, shift_sum, w_in_sum, b_in_sum, w_out_sum, scale_sum)
    )
    factor = 1.0 / math.sqrt(height * lax.axis_size("row") * breadth * lax.axis_size("col"))
    return (
        block_out,
        image_grad,
        factor * kernel_sum,
        factor * bias_sum,
        factor * gain_sum,
        factor * shift_sum,
        factor * w_in_sum,
        factor * b_in_sum,
        factor * w_out_sum,
        factor * scale_sum,
    )


def solution(mesh):
    in_specs = (
        P(None, "row", "col"),
        P(None, "row", "col"),
        P(),
        P(),
        P(),
        P(),
        P(),
        P(),
        P(),
        P(),
    )
    out_specs = (
        P(None, "row", "col"),
        P(None, "row", "col"),
        P(),
        P(),
        P(),
        P(),
        P(),
        P(),
        P(),
        P(),
    )
    return jax.shard_map(local, mesh=mesh, in_specs=in_specs, out_specs=out_specs, check_vma=False)
```

```python
import math

import jax
import jax.numpy as jnp
from jax import lax
from jax.sharding import PartitionSpec as P


def padded_2(block, sides, width):
    for axis, dim in sides:
        count = lax.axis_size(axis)
        forward = [(i, i + 1) for i in range(count - 1)]
        backward = [(target, source) for source, target in forward]
        low = lax.ppermute(
            lax.slice_in_dim(block, block.shape[dim] - width, None, axis=dim), axis, forward
        )
        high = lax.ppermute(lax.slice_in_dim(block, 0, width, axis=dim), axis, backward)
        block = jnp.concatenate([low, block, high], axis=dim)
    return block


def from_behind(value, axis, steps):
    count = lax.axis_size(axis)
    initial, last = (max(0, -steps), min(count, count - steps))
    return lax.ppermute(value, axis, [(source, source + steps) for source in range(initial, last)])


def conv_seven(padded, kernel):
    height = padded.shape[1] - 6
    breadth = padded.shape[2] - 6
    summed = jnp.zeros((padded.shape[0], height, breadth), jnp.float32)
    for row_step in range(7):
        for col_step in range(7):
            summed = (
                summed
                + kernel[:, row_step, col_step][:, None, None]
                * padded[:, row_step : row_step + height, col_step : col_step + breadth]
            )
    return summed


def kernel_terms(conv_grad, padded):
    height, breadth = (conv_grad.shape[1], conv_grad.shape[2])
    pieces = []
    for row_step in range(7):
        for col_step in range(7):
            pieces.append(
                jnp.sum(
                    conv_grad
                    * padded[:, row_step : row_step + height, col_step : col_step + breadth],
                    axis=(1, 2),
                )
            )
    return jnp.stack(pieces, axis=1).reshape(conv_grad.shape[0], 7, 7)


def xor_partner(value, axis, mask):
    return lax.ppermute(value, axis, [(i, i ^ mask) for i in range(lax.axis_size(axis))])


def butterfly_sum(parts, halving=(("col", 1), ("col", 2))):
    shapes = [p.shape for p in parts]
    flat = jnp.concatenate([p.reshape(-1) for p in parts])
    total = flat.shape[0]
    unit = 2 ** len(halving)
    flat = jnp.pad(flat, (0, -total % unit))
    doubling = []
    for axis in ("col", "row"):
        mask = 1
        while mask < lax.axis_size(axis):
            if (axis, mask) not in halving:
                doubling.append((axis, mask))
            mask *= 2
    sides = []
    for axis, mask in halving:
        half = flat.shape[0] // 2
        side = (lax.axis_index(axis) // mask) % 2
        keep = lax.dynamic_slice_in_dim(flat, side * half, half)
        send = lax.dynamic_slice_in_dim(flat, (1 - side) * half, half)
        flat = keep + xor_partner(send, axis, mask)
        sides.append(side)
    for axis, mask in doubling:
        flat = flat + xor_partner(flat, axis, mask)
    for (axis, mask), side in zip(reversed(halving), reversed(sides)):
        other = xor_partner(flat, axis, mask)
        flat = jnp.where(side == 0, jnp.concatenate([flat, other]), jnp.concatenate([other, flat]))
    out, start = [], 0
    for shape in shapes:
        size = math.prod(shape)
        out.append(flat[start : start + size].reshape(shape))
        start += size
    return tuple(out)


def product(form, left, right):
    return jnp.einsum(form, left, right, preferred_element_type=jnp.float32)


def mixing(conv_flat, image_flat, cotan_flat, ln_gain, ln_bias, w_in, b_in, w_out, layer_scale):
    average = jnp.mean(conv_flat, axis=0, keepdims=True)
    centred = conv_flat - average
    spread = jnp.mean(centred * centred, axis=0, keepdims=True)
    inverse = lax.rsqrt(spread + 1e-06)
    normed = centred * inverse
    ln_out = (normed * ln_gain[:, None] + ln_bias[:, None]).astype(jnp.bfloat16)
    pre_act = product("ch,cp->hp", w_in, ln_out) + b_in[:, None]
    act_out, gelu_pull = jax.vjp(jax.nn.gelu, pre_act)
    activ = act_out.astype(jnp.bfloat16)
    branch = product("hc,hp->cp", w_out, activ)
    scale_col = layer_scale[:, None]
    block_out = (image_flat.astype(jnp.float32) + scale_col * branch).astype(jnp.bfloat16)
    upstream = cotan_flat.astype(jnp.float32)
    scale_sum = jnp.sum(upstream * branch, axis=1)
    branch_grad = (scale_col * upstream).astype(jnp.bfloat16)
    w_out_sum = product("hp,cp->hc", activ, branch_grad)
    act_grad = product("hc,cp->hp", w_out, branch_grad)
    pre_grad = gelu_pull(act_grad)[0].astype(jnp.bfloat16)
    b_in_sum = jnp.sum(pre_grad.astype(jnp.float32), axis=1)
    w_in_sum = product("cp,hp->ch", ln_out, pre_grad)
    ln_grad = product("ch,hp->cp", w_in, pre_grad)
    gain_sum = jnp.sum(ln_grad * normed, axis=1)
    shift_sum = jnp.sum(ln_grad, axis=1)
    normed_grad = ln_grad * ln_gain[:, None]
    conv_grad = inverse * (
        normed_grad
        - jnp.mean(normed_grad, axis=0, keepdims=True)
        - normed * jnp.mean(normed_grad * normed, axis=0, keepdims=True)
    )
    return (block_out, conv_grad, (gain_sum, shift_sum, w_in_sum, b_in_sum, w_out_sum, scale_sum))


def local(image, cotangent, dw_kernel, dw_bias, ln_gain, ln_bias, w_in, b_in, w_out, layer_scale):
    channels, height, breadth = image.shape
    pixels = height * breadth
    padded = padded_2(image, (("col", 2), ("row", 1)), 3)
    conv_out = conv_seven(padded, dw_kernel) + dw_bias[:, None, None]
    block_flat, grad_flat, sums = mixing(
        conv_out.reshape(channels, pixels),
        image.reshape(channels, pixels),
        cotangent.reshape(channels, pixels),
        ln_gain,
        ln_bias,
        w_in,
        b_in,
        w_out,
        layer_scale,
    )
    gain_sum, shift_sum, w_in_sum, b_in_sum, w_out_sum, scale_sum = sums
    block_out = block_flat.reshape(channels, height, breadth)
    conv_grad = grad_flat.reshape(channels, height, breadth)
    flipped = dw_kernel[:, ::-1, ::-1]
    grad_col = padded_2(conv_grad, (("col", 2),), 3)
    grad_rows = padded_2(grad_col.astype(jnp.bfloat16), (("row", 1),), 3).astype(jnp.float32)
    grad_padded = jnp.concatenate(
        [grad_rows[:, :3, :], grad_col, grad_rows[:, height + 3 :, :]], axis=1
    )
    back = conv_seven(grad_padded, flipped)
    image_grad = (cotangent.astype(jnp.float32) + back).astype(jnp.bfloat16)
    kernel_sum = kernel_terms(conv_grad, padded)
    bias_sum = jnp.sum(conv_grad, axis=(1, 2))
    kernel_sum, bias_sum, gain_sum, shift_sum, w_in_sum, b_in_sum, w_out_sum, scale_sum = butterfly_sum(
        (kernel_sum, bias_sum, gain_sum, shift_sum, w_in_sum, b_in_sum, w_out_sum, scale_sum)
    )
    factor = 1.0 / math.sqrt(height * lax.axis_size("row") * breadth * lax.axis_size("col"))
    return (
        block_out,
        image_grad,
        factor * kernel_sum,
        factor * bias_sum,
        factor * gain_sum,
        factor * shift_sum,
        factor * w_in_sum,
        factor * b_in_sum,
        factor * w_out_sum,
        factor * scale_sum,
    )


def solution(mesh):
    in_specs = (
        P(None, "row", "col"),
        P(None, "row", "col"),
        P(),
        P(),
        P(),
        P(),
        P(),
        P(),
        P(),
        P(),
    )
    out_specs = (
        P(None, "row", "col"),
        P(None, "row", "col"),
        P(),
        P(),
        P(),
        P(),
        P(),
        P(),
        P(),
        P(),
    )
    return jax.shard_map(local, mesh=mesh, in_specs=in_specs, out_specs=out_specs, check_vma=False)
```

```python
import math

import jax
import jax.numpy as jnp
from jax import lax
from jax.sharding import PartitionSpec as P


def padded_2(block, sides, width):
    for axis, dim in sides:
        count = lax.axis_size(axis)
        forward = [(i, i + 1) for i in range(count - 1)]
        backward = [(target, source) for source, target in forward]
        low = lax.ppermute(
            lax.slice_in_dim(block, block.shape[dim] - width, None, axis=dim), axis, forward
        )
        high = lax.ppermute(lax.slice_in_dim(block, 0, width, axis=dim), axis, backward)
        block = jnp.concatenate([low, block, high], axis=dim)
    return block


def from_behind(value, axis, steps):
    count = lax.axis_size(axis)
    initial, last = (max(0, -steps), min(count, count - steps))
    return lax.ppermute(value, axis, [(source, source + steps) for source in range(initial, last)])


def conv_seven(padded, kernel):
    height = padded.shape[1] - 6
    breadth = padded.shape[2] - 6
    summed = jnp.zeros((padded.shape[0], height, breadth), jnp.float32)
    for row_step in range(7):
        for col_step in range(7):
            summed = (
                summed
                + kernel[:, row_step, col_step][:, None, None]
                * padded[:, row_step : row_step + height, col_step : col_step + breadth]
            )
    return summed


def kernel_terms(conv_grad, padded):
    height, breadth = (conv_grad.shape[1], conv_grad.shape[2])
    pieces = []
    for row_step in range(7):
        for col_step in range(7):
            pieces.append(
                jnp.sum(
                    conv_grad
                    * padded[:, row_step : row_step + height, col_step : col_step + breadth],
                    axis=(1, 2),
                )
            )
    return jnp.stack(pieces, axis=1).reshape(conv_grad.shape[0], 7, 7)


def xor_partner(value, axis, mask):
    return lax.ppermute(value, axis, [(i, i ^ mask) for i in range(lax.axis_size(axis))])


def butterfly_sum(parts, halving=(("col", 1), ("col", 2))):
    shapes = [p.shape for p in parts]
    flat = jnp.concatenate([p.reshape(-1) for p in parts])
    total = flat.shape[0]
    unit = 2 ** len(halving)
    flat = jnp.pad(flat, (0, -total % unit))
    doubling = []
    for axis in ("col", "row"):
        mask = 1
        while mask < lax.axis_size(axis):
            if (axis, mask) not in halving:
                doubling.append((axis, mask))
            mask *= 2
    sides = []
    for axis, mask in halving:
        half = flat.shape[0] // 2
        side = (lax.axis_index(axis) // mask) % 2
        keep = lax.dynamic_slice_in_dim(flat, side * half, half)
        send = lax.dynamic_slice_in_dim(flat, (1 - side) * half, half)
        flat = keep + xor_partner(send, axis, mask)
        sides.append(side)
    for axis, mask in doubling:
        flat = flat + xor_partner(flat, axis, mask)
    for (axis, mask), side in zip(reversed(halving), reversed(sides)):
        other = xor_partner(flat, axis, mask)
        flat = jnp.where(side == 0, jnp.concatenate([flat, other]), jnp.concatenate([other, flat]))
    out, start = [], 0
    for shape in shapes:
        size = math.prod(shape)
        out.append(flat[start : start + size].reshape(shape))
        start += size
    return tuple(out)


def product(form, left, right):
    return jnp.einsum(form, left, right, preferred_element_type=jnp.float32)


def mixing(conv_flat, image_flat, cotan_flat, ln_gain, ln_bias, w_in, b_in, w_out, layer_scale):
    average = jnp.mean(conv_flat, axis=0, keepdims=True)
    centred = conv_flat - average
    spread = jnp.mean(centred * centred, axis=0, keepdims=True)
    inverse = lax.rsqrt(spread + 1e-06)
    normed = centred * inverse
    ln_out = (normed * ln_gain[:, None] + ln_bias[:, None]).astype(jnp.bfloat16)
    pre_act = product("ch,cp->hp", w_in, ln_out) + b_in[:, None]
    act_out, gelu_pull = jax.vjp(jax.nn.gelu, pre_act)
    activ = act_out.astype(jnp.bfloat16)
    branch = product("hc,hp->cp", w_out, activ)
    scale_col = layer_scale[:, None]
    block_out = (image_flat.astype(jnp.float32) + scale_col * branch).astype(jnp.bfloat16)
    upstream = cotan_flat.astype(jnp.float32)
    scale_sum = jnp.sum(upstream * branch, axis=1)
    branch_grad = (scale_col * upstream).astype(jnp.bfloat16)
    w_out_sum = product("hp,cp->hc", activ, branch_grad)
    act_grad = product("hc,cp->hp", w_out, branch_grad)
    pre_grad = gelu_pull(act_grad)[0].astype(jnp.bfloat16)
    b_in_sum = jnp.sum(pre_grad.astype(jnp.float32), axis=1)
    w_in_sum = product("cp,hp->ch", ln_out, pre_grad)
    ln_grad = product("ch,hp->cp", w_in, pre_grad)
    gain_sum = jnp.sum(ln_grad * normed, axis=1)
    shift_sum = jnp.sum(ln_grad, axis=1)
    normed_grad = ln_grad * ln_gain[:, None]
    conv_grad = inverse * (
        normed_grad
        - jnp.mean(normed_grad, axis=0, keepdims=True)
        - normed * jnp.mean(normed_grad * normed, axis=0, keepdims=True)
    )
    return (block_out, conv_grad, (gain_sum, shift_sum, w_in_sum, b_in_sum, w_out_sum, scale_sum))


def local(image, cotangent, dw_kernel, dw_bias, ln_gain, ln_bias, w_in, b_in, w_out, layer_scale):
    channels, height, breadth = image.shape
    pixels = height * breadth
    padded_c = padded_2(image, (("col", 2),), 3)
    count = lax.axis_size("row")
    forward = [(i, i + 1) for i in range(count - 1)]
    backward = [(target, source) for source, target in forward]
    above = lax.ppermute(padded_c[:, height - 3 :, :], "row", forward)
    below = lax.ppermute(padded_c[:, :3, :], "row", backward)
    padded = jnp.concatenate([above, padded_c, below], axis=1)
    bias = dw_bias[:, None, None]
    conv_mid = conv_seven(padded_c, dw_kernel) + bias
    conv_top = conv_seven(jnp.concatenate([above, padded_c[:, :6, :]], axis=1), dw_kernel) + bias
    conv_bot = (
        conv_seven(jnp.concatenate([padded_c[:, height - 6 :, :], below], axis=1), dw_kernel) + bias
    )
    params = (ln_gain, ln_bias, w_in, b_in, w_out, layer_scale)

    def flat(field):
        return field.reshape(channels, -1)

    def edges(field):
        return jnp.concatenate([field[:, :3, :], field[:, height - 3 :, :]], axis=1)

    mid_out, mid_grad, mid_sums = mixing(
        flat(conv_mid), flat(image[:, 3 : height - 3, :]), flat(cotangent[:, 3 : height - 3, :]), *params
    )
    edge_out, edge_grad, edge_sums = mixing(
        flat(jnp.concatenate([conv_top, conv_bot], axis=1)), flat(edges(image)), flat(edges(cotangent)), *params
    )
    sums = tuple(x + y for x, y in zip(edge_sums, mid_sums))
    gain_sum, shift_sum, w_in_sum, b_in_sum, w_out_sum, scale_sum = sums

    def assemble(edge_flat, mid_flat):
        edge_rows = edge_flat.reshape(channels, 6, breadth)
        mid_rows = mid_flat.reshape(channels, height - 6, breadth)
        return jnp.concatenate([edge_rows[:, :3], mid_rows, edge_rows[:, 3:]], axis=1)

    block_out = assemble(edge_out, mid_out)
    conv_grad = assemble(edge_grad, mid_grad)
    flipped = dw_kernel[:, ::-1, ::-1]
    grad_col = padded_2(conv_grad, (("col", 2),), 3)
    grad_rows = padded_2(grad_col.astype(jnp.bfloat16), (("row", 1),), 3).astype(jnp.float32)
    grad_padded = jnp.concatenate(
        [grad_rows[:, :3, :], grad_col, grad_rows[:, height + 3 :, :]], axis=1
    )
    back = conv_seven(grad_padded, flipped)
    image_grad = (cotangent.astype(jnp.float32) + back).astype(jnp.bfloat16)
    kernel_sum = kernel_terms(conv_grad, padded)
    bias_sum = jnp.sum(conv_grad, axis=(1, 2))
    kernel_sum, bias_sum, gain_sum, shift_sum, w_in_sum, b_in_sum, w_out_sum, scale_sum = butterfly_sum(
        (kernel_sum, bias_sum, gain_sum, shift_sum, w_in_sum, b_in_sum, w_out_sum, scale_sum)
    )
    factor = 1.0 / math.sqrt(height * lax.axis_size("row") * breadth * lax.axis_size("col"))
    return (
        block_out,
        image_grad,
        factor * kernel_sum,
        factor * bias_sum,
        factor * gain_sum,
        factor * shift_sum,
        factor * w_in_sum,
        factor * b_in_sum,
        factor * w_out_sum,
        factor * scale_sum,
    )


def solution(mesh):
    in_specs = (
        P(None, "row", "col"),
        P(None, "row", "col"),
        P(),
        P(),
        P(),
        P(),
        P(),
        P(),
        P(),
        P(),
    )
    out_specs = (
        P(None, "row", "col"),
        P(None, "row", "col"),
        P(),
        P(),
        P(),
        P(),
        P(),
        P(),
        P(),
        P(),
    )
    return jax.shard_map(local, mesh=mesh, in_specs=in_specs, out_specs=out_specs, check_vma=False)
```

```python
import math

import jax
import jax.numpy as jnp
from jax import lax
from jax.sharding import PartitionSpec as P


def padded_2(block, sides, width):
    for axis, dim in sides:
        count = lax.axis_size(axis)
        forward = [(i, i + 1) for i in range(count - 1)]
        backward = [(target, source) for source, target in forward]
        low = lax.ppermute(
            lax.slice_in_dim(block, block.shape[dim] - width, None, axis=dim), axis, forward
        )
        high = lax.ppermute(lax.slice_in_dim(block, 0, width, axis=dim), axis, backward)
        block = jnp.concatenate([low, block, high], axis=dim)
    return block


def from_behind(value, axis, steps):
    count = lax.axis_size(axis)
    initial, last = (max(0, -steps), min(count, count - steps))
    return lax.ppermute(value, axis, [(source, source + steps) for source in range(initial, last)])


def conv_seven(padded, kernel):
    height = padded.shape[1] - 6
    breadth = padded.shape[2] - 6
    summed = jnp.zeros((padded.shape[0], height, breadth), jnp.float32)
    for row_step in range(7):
        for col_step in range(7):
            summed = (
                summed
                + kernel[:, row_step, col_step][:, None, None]
                * padded[:, row_step : row_step + height, col_step : col_step + breadth]
            )
    return summed


def kernel_terms(conv_grad, padded):
    height, breadth = (conv_grad.shape[1], conv_grad.shape[2])
    pieces = []
    for row_step in range(7):
        for col_step in range(7):
            pieces.append(
                jnp.sum(
                    conv_grad
                    * padded[:, row_step : row_step + height, col_step : col_step + breadth],
                    axis=(1, 2),
                )
            )
    return jnp.stack(pieces, axis=1).reshape(conv_grad.shape[0], 7, 7)


def xor_partner(value, axis, mask):
    return lax.ppermute(value, axis, [(i, i ^ mask) for i in range(lax.axis_size(axis))])


def butterfly_sum(parts, halving=(("col", 1), ("col", 2))):
    shapes = [p.shape for p in parts]
    flat = jnp.concatenate([p.reshape(-1) for p in parts])
    total = flat.shape[0]
    unit = 2 ** len(halving)
    flat = jnp.pad(flat, (0, -total % unit))
    doubling = []
    for axis in ("col", "row"):
        mask = 1
        while mask < lax.axis_size(axis):
            if (axis, mask) not in halving:
                doubling.append((axis, mask))
            mask *= 2
    sides = []
    for axis, mask in halving:
        half = flat.shape[0] // 2
        side = (lax.axis_index(axis) // mask) % 2
        keep = lax.dynamic_slice_in_dim(flat, side * half, half)
        send = lax.dynamic_slice_in_dim(flat, (1 - side) * half, half)
        flat = keep + xor_partner(send, axis, mask)
        sides.append(side)
    for axis, mask in doubling:
        flat = flat + xor_partner(flat, axis, mask)
    for (axis, mask), side in zip(reversed(halving), reversed(sides)):
        other = xor_partner(flat, axis, mask)
        flat = jnp.where(side == 0, jnp.concatenate([flat, other]), jnp.concatenate([other, flat]))
    out, start = [], 0
    for shape in shapes:
        size = math.prod(shape)
        out.append(flat[start : start + size].reshape(shape))
        start += size
    return tuple(out)


def product(form, left, right):
    return jnp.einsum(form, left, right, preferred_element_type=jnp.float32)


def mixing(conv_flat, image_flat, cotan_flat, ln_gain, ln_bias, w_in, b_in, w_out, layer_scale):
    average = jnp.mean(conv_flat, axis=0, keepdims=True)
    centred = conv_flat - average
    spread = jnp.mean(centred * centred, axis=0, keepdims=True)
    inverse = lax.rsqrt(spread + 1e-06)
    normed = centred * inverse
    ln_out = (normed * ln_gain[:, None] + ln_bias[:, None]).astype(jnp.bfloat16)
    pre_act = product("ch,cp->hp", w_in, ln_out) + b_in[:, None]
    act_out, gelu_pull = jax.vjp(jax.nn.gelu, pre_act)
    activ = act_out.astype(jnp.bfloat16)
    branch = product("hc,hp->cp", w_out, activ)
    scale_col = layer_scale[:, None]
    block_out = (image_flat.astype(jnp.float32) + scale_col * branch).astype(jnp.bfloat16)
    upstream = cotan_flat.astype(jnp.float32)
    scale_sum = jnp.sum(upstream * branch, axis=1)
    branch_grad = (scale_col * upstream).astype(jnp.bfloat16)
    w_out_sum = product("hp,cp->hc", activ, branch_grad)
    act_grad = product("hc,cp->hp", w_out, branch_grad)
    pre_grad = gelu_pull(act_grad)[0].astype(jnp.bfloat16)
    b_in_sum = jnp.sum(pre_grad.astype(jnp.float32), axis=1)
    w_in_sum = product("cp,hp->ch", ln_out, pre_grad)
    ln_grad = product("ch,hp->cp", w_in, pre_grad)
    gain_sum = jnp.sum(ln_grad * normed, axis=1)
    shift_sum = jnp.sum(ln_grad, axis=1)
    normed_grad = ln_grad * ln_gain[:, None]
    conv_grad = inverse * (
        normed_grad
        - jnp.mean(normed_grad, axis=0, keepdims=True)
        - normed * jnp.mean(normed_grad * normed, axis=0, keepdims=True)
    )
    return (block_out, conv_grad, (gain_sum, shift_sum, w_in_sum, b_in_sum, w_out_sum, scale_sum))


def local(image, cotangent, dw_kernel, dw_bias, ln_gain, ln_bias, w_in, b_in, w_out, layer_scale):
    channels, height, breadth = image.shape
    pixels = height * breadth
    count = lax.axis_size("row")
    forward = [(i, i + 1) for i in range(count - 1)]
    backward = [(target, source) for source, target in forward]
    above_raw = lax.ppermute(image[:, height - 3 :, :], "row", forward)
    below_raw = lax.ppermute(image[:, :3, :], "row", backward)
    padded_c = padded_2(image, (("col", 2),), 3)
    strips = padded_2(jnp.concatenate([above_raw, below_raw], axis=1), (("col", 2),), 3)
    above, below = strips[:, :3, :], strips[:, 3:, :]
    padded = jnp.concatenate([above, padded_c, below], axis=1)
    bias = dw_bias[:, None, None]
    conv_mid = conv_seven(padded_c, dw_kernel) + bias
    conv_top = conv_seven(jnp.concatenate([above, padded_c[:, :6, :]], axis=1), dw_kernel) + bias
    conv_bot = (
        conv_seven(jnp.concatenate([padded_c[:, height - 6 :, :], below], axis=1), dw_kernel) + bias
    )
    params = (ln_gain, ln_bias, w_in, b_in, w_out, layer_scale)

    def flat(field):
        return field.reshape(channels, -1)

    def edges(field):
        return jnp.concatenate([field[:, :3, :], field[:, height - 3 :, :]], axis=1)

    mid_out, mid_grad, mid_sums = mixing(
        flat(conv_mid), flat(image[:, 3 : height - 3, :]), flat(cotangent[:, 3 : height - 3, :]), *params
    )
    edge_out, edge_grad, edge_sums = mixing(
        flat(jnp.concatenate([conv_top, conv_bot], axis=1)), flat(edges(image)), flat(edges(cotangent)), *params
    )
    sums = tuple(x + y for x, y in zip(edge_sums, mid_sums))
    gain_sum, shift_sum, w_in_sum, b_in_sum, w_out_sum, scale_sum = sums

    def assemble(edge_flat, mid_flat):
        edge_rows = edge_flat.reshape(channels, 6, breadth)
        mid_rows = mid_flat.reshape(channels, height - 6, breadth)
        return jnp.concatenate([edge_rows[:, :3], mid_rows, edge_rows[:, 3:]], axis=1)

    block_out = assemble(edge_out, mid_out)
    conv_grad = assemble(edge_grad, mid_grad)
    flipped = dw_kernel[:, ::-1, ::-1]
    grad_col = padded_2(conv_grad, (("col", 2),), 3)
    grad_rows = padded_2(grad_col.astype(jnp.bfloat16), (("row", 1),), 3).astype(jnp.float32)
    grad_padded = jnp.concatenate(
        [grad_rows[:, :3, :], grad_col, grad_rows[:, height + 3 :, :]], axis=1
    )
    back = conv_seven(grad_padded, flipped)
    image_grad = (cotangent.astype(jnp.float32) + back).astype(jnp.bfloat16)
    kernel_sum = kernel_terms(conv_grad, padded)
    bias_sum = jnp.sum(conv_grad, axis=(1, 2))
    kernel_sum, bias_sum, gain_sum, shift_sum, w_in_sum, b_in_sum, w_out_sum, scale_sum = butterfly_sum(
        (kernel_sum, bias_sum, gain_sum, shift_sum, w_in_sum, b_in_sum, w_out_sum, scale_sum)
    )
    factor = 1.0 / math.sqrt(height * lax.axis_size("row") * breadth * lax.axis_size("col"))
    return (
        block_out,
        image_grad,
        factor * kernel_sum,
        factor * bias_sum,
        factor * gain_sum,
        factor * shift_sum,
        factor * w_in_sum,
        factor * b_in_sum,
        factor * w_out_sum,
        factor * scale_sum,
    )


def solution(mesh):
    in_specs = (
        P(None, "row", "col"),
        P(None, "row", "col"),
        P(),
        P(),
        P(),
        P(),
        P(),
        P(),
        P(),
        P(),
    )
    out_specs = (
        P(None, "row", "col"),
        P(None, "row", "col"),
        P(),
        P(),
        P(),
        P(),
        P(),
        P(),
        P(),
        P(),
    )
    return jax.shard_map(local, mesh=mesh, in_specs=in_specs, out_specs=out_specs, check_vma=False)
```

```python
import math

import jax
import jax.numpy as jnp
from jax import lax
from jax.sharding import PartitionSpec as P


def padded_2(block, sides, width):
    for axis, dim in sides:
        count = lax.axis_size(axis)
        forward = [(i, i + 1) for i in range(count - 1)]
        backward = [(target, source) for source, target in forward]
        low = lax.ppermute(
            lax.slice_in_dim(block, block.shape[dim] - width, None, axis=dim), axis, forward
        )
        high = lax.ppermute(lax.slice_in_dim(block, 0, width, axis=dim), axis, backward)
        block = jnp.concatenate([low, block, high], axis=dim)
    return block


def padded_one_round(block, width):
    cols, rows = lax.axis_size("col"), lax.axis_size("row")
    height, breadth = block.shape[1], block.shape[2]
    top, bottom = slice(0, width), slice(height - width, height)
    first, last = slice(0, width), slice(breadth - width, breadth)

    def moved(piece, dc, dr):
        pairs = [
            (c * rows + r, (c + dc) * rows + (r + dr))
            for c in range(cols)
            for r in range(rows)
            if 0 <= c + dc < cols and 0 <= r + dr < rows
        ]
        return lax.ppermute(piece, ("col", "row"), pairs)

    above = lax.ppermute(block[:, bottom, :], "row", [(i, i + 1) for i in range(rows - 1)])
    below = lax.ppermute(block[:, top, :], "row", [(i + 1, i) for i in range(rows - 1)])
    left = lax.ppermute(block[:, :, last], "col", [(i, i + 1) for i in range(cols - 1)])
    right = lax.ppermute(block[:, :, first], "col", [(i + 1, i) for i in range(cols - 1)])
    top_left = moved(block[:, bottom, last], 1, 1)
    top_right = moved(block[:, bottom, first], -1, 1)
    bottom_left = moved(block[:, top, last], 1, -1)
    bottom_right = moved(block[:, top, first], -1, -1)
    upper = jnp.concatenate([top_left, above, top_right], axis=2)
    middle = jnp.concatenate([left, block, right], axis=2)
    lower = jnp.concatenate([bottom_left, below, bottom_right], axis=2)
    return jnp.concatenate([upper, middle, lower], axis=1)


def from_behind(value, axis, steps):
    count = lax.axis_size(axis)
    initial, last = (max(0, -steps), min(count, count - steps))
    return lax.ppermute(value, axis, [(source, source + steps) for source in range(initial, last)])


def conv_seven(padded, kernel):
    height = padded.shape[1] - 6
    breadth = padded.shape[2] - 6
    summed = jnp.zeros((padded.shape[0], height, breadth), jnp.float32)
    for row_step in range(7):
        for col_step in range(7):
            summed = (
                summed
                + kernel[:, row_step, col_step][:, None, None]
                * padded[:, row_step : row_step + height, col_step : col_step + breadth]
            )
    return summed


def kernel_terms(conv_grad, padded):
    height, breadth = (conv_grad.shape[1], conv_grad.shape[2])
    pieces = []
    for row_step in range(7):
        for col_step in range(7):
            pieces.append(
                jnp.sum(
                    conv_grad
                    * padded[:, row_step : row_step + height, col_step : col_step + breadth],
                    axis=(1, 2),
                )
            )
    return jnp.stack(pieces, axis=1).reshape(conv_grad.shape[0], 7, 7)


def xor_partner(value, axis, mask):
    return lax.ppermute(value, axis, [(i, i ^ mask) for i in range(lax.axis_size(axis))])


def butterfly_sum(parts, halving=(("col", 1), ("col", 2))):
    shapes = [p.shape for p in parts]
    flat = jnp.concatenate([p.reshape(-1) for p in parts])
    total = flat.shape[0]
    unit = 2 ** len(halving)
    flat = jnp.pad(flat, (0, -total % unit))
    doubling = []
    for axis in ("col", "row"):
        mask = 1
        while mask < lax.axis_size(axis):
            if (axis, mask) not in halving:
                doubling.append((axis, mask))
            mask *= 2
    sides = []
    for axis, mask in halving:
        half = flat.shape[0] // 2
        side = (lax.axis_index(axis) // mask) % 2
        keep = lax.dynamic_slice_in_dim(flat, side * half, half)
        send = lax.dynamic_slice_in_dim(flat, (1 - side) * half, half)
        flat = keep + xor_partner(send, axis, mask)
        sides.append(side)
    for axis, mask in doubling:
        flat = flat + xor_partner(flat, axis, mask)
    for (axis, mask), side in zip(reversed(halving), reversed(sides)):
        other = xor_partner(flat, axis, mask)
        flat = jnp.where(side == 0, jnp.concatenate([flat, other]), jnp.concatenate([other, flat]))
    out, start = [], 0
    for shape in shapes:
        size = math.prod(shape)
        out.append(flat[start : start + size].reshape(shape))
        start += size
    return tuple(out)


def product(form, left, right):
    return jnp.einsum(form, left, right, preferred_element_type=jnp.float32)


def mixing(conv_flat, image_flat, cotan_flat, ln_gain, ln_bias, w_in, b_in, w_out, layer_scale):
    average = jnp.mean(conv_flat, axis=0, keepdims=True)
    centred = conv_flat - average
    spread = jnp.mean(centred * centred, axis=0, keepdims=True)
    inverse = lax.rsqrt(spread + 1e-06)
    normed = centred * inverse
    ln_out = (normed * ln_gain[:, None] + ln_bias[:, None]).astype(jnp.bfloat16)
    pre_act = product("ch,cp->hp", w_in, ln_out) + b_in[:, None]
    act_out, gelu_pull = jax.vjp(jax.nn.gelu, pre_act)
    activ = act_out.astype(jnp.bfloat16)
    branch = product("hc,hp->cp", w_out, activ)
    scale_col = layer_scale[:, None]
    block_out = (image_flat.astype(jnp.float32) + scale_col * branch).astype(jnp.bfloat16)
    upstream = cotan_flat.astype(jnp.float32)
    scale_sum = jnp.sum(upstream * branch, axis=1)
    branch_grad = (scale_col * upstream).astype(jnp.bfloat16)
    w_out_sum = product("hp,cp->hc", activ, branch_grad)
    act_grad = product("hc,cp->hp", w_out, branch_grad)
    pre_grad = gelu_pull(act_grad)[0].astype(jnp.bfloat16)
    b_in_sum = jnp.sum(pre_grad.astype(jnp.float32), axis=1)
    w_in_sum = product("cp,hp->ch", ln_out, pre_grad)
    ln_grad = product("ch,hp->cp", w_in, pre_grad)
    gain_sum = jnp.sum(ln_grad * normed, axis=1)
    shift_sum = jnp.sum(ln_grad, axis=1)
    normed_grad = ln_grad * ln_gain[:, None]
    conv_grad = inverse * (
        normed_grad
        - jnp.mean(normed_grad, axis=0, keepdims=True)
        - normed * jnp.mean(normed_grad * normed, axis=0, keepdims=True)
    )
    return (block_out, conv_grad, (gain_sum, shift_sum, w_in_sum, b_in_sum, w_out_sum, scale_sum))


def local(image, cotangent, dw_kernel, dw_bias, ln_gain, ln_bias, w_in, b_in, w_out, layer_scale):
    channels, height, breadth = image.shape
    pixels = height * breadth
    padded = padded_one_round(image, 3)
    conv_out = conv_seven(padded, dw_kernel) + dw_bias[:, None, None]
    block_flat, grad_flat, sums = mixing(
        conv_out.reshape(channels, pixels),
        image.reshape(channels, pixels),
        cotangent.reshape(channels, pixels),
        ln_gain,
        ln_bias,
        w_in,
        b_in,
        w_out,
        layer_scale,
    )
    gain_sum, shift_sum, w_in_sum, b_in_sum, w_out_sum, scale_sum = sums
    block_out = block_flat.reshape(channels, height, breadth)
    conv_grad = grad_flat.reshape(channels, height, breadth)
    flipped = dw_kernel[:, ::-1, ::-1]
    grad_col = padded_2(conv_grad, (("col", 2),), 3)
    grad_rows = padded_2(grad_col.astype(jnp.bfloat16), (("row", 1),), 3).astype(jnp.float32)
    grad_padded = jnp.concatenate(
        [grad_rows[:, :3, :], grad_col, grad_rows[:, height + 3 :, :]], axis=1
    )
    back = conv_seven(grad_padded, flipped)
    image_grad = (cotangent.astype(jnp.float32) + back).astype(jnp.bfloat16)
    kernel_sum = kernel_terms(conv_grad, padded)
    bias_sum = jnp.sum(conv_grad, axis=(1, 2))
    kernel_sum, bias_sum, gain_sum, shift_sum, w_in_sum, b_in_sum, w_out_sum, scale_sum = butterfly_sum(
        (kernel_sum, bias_sum, gain_sum, shift_sum, w_in_sum, b_in_sum, w_out_sum, scale_sum)
    )
    factor = 1.0 / math.sqrt(height * lax.axis_size("row") * breadth * lax.axis_size("col"))
    return (
        block_out,
        image_grad,
        factor * kernel_sum,
        factor * bias_sum,
        factor * gain_sum,
        factor * shift_sum,
        factor * w_in_sum,
        factor * b_in_sum,
        factor * w_out_sum,
        factor * scale_sum,
    )


def solution(mesh):
    in_specs = (
        P(None, "row", "col"),
        P(None, "row", "col"),
        P(),
        P(),
        P(),
        P(),
        P(),
        P(),
        P(),
        P(),
    )
    out_specs = (
        P(None, "row", "col"),
        P(None, "row", "col"),
        P(),
        P(),
        P(),
        P(),
        P(),
        P(),
        P(),
        P(),
    )
    return jax.shard_map(local, mesh=mesh, in_specs=in_specs, out_specs=out_specs, check_vma=False)
```

```python
import math

import jax
import jax.numpy as jnp
from jax import lax
from jax.sharding import PartitionSpec as P


def padded_2(block, sides, width):
    for axis, dim in sides:
        count = lax.axis_size(axis)
        forward = [(i, i + 1) for i in range(count - 1)]
        backward = [(target, source) for source, target in forward]
        low = lax.ppermute(
            lax.slice_in_dim(block, block.shape[dim] - width, None, axis=dim), axis, forward
        )
        high = lax.ppermute(lax.slice_in_dim(block, 0, width, axis=dim), axis, backward)
        block = jnp.concatenate([low, block, high], axis=dim)
    return block


def from_behind(value, axis, steps):
    count = lax.axis_size(axis)
    initial, last = (max(0, -steps), min(count, count - steps))
    return lax.ppermute(value, axis, [(source, source + steps) for source in range(initial, last)])


def conv_seven(padded, kernel):
    height = padded.shape[1] - 6
    breadth = padded.shape[2] - 6
    summed = jnp.zeros((padded.shape[0], height, breadth), jnp.float32)
    for row_step in range(7):
        for col_step in range(7):
            summed = (
                summed
                + kernel[:, row_step, col_step][:, None, None]
                * padded[:, row_step : row_step + height, col_step : col_step + breadth]
            )
    return summed


def kernel_terms(conv_grad, padded):
    height, breadth = (conv_grad.shape[1], conv_grad.shape[2])
    pieces = []
    for row_step in range(7):
        for col_step in range(7):
            pieces.append(
                jnp.sum(
                    conv_grad
                    * padded[:, row_step : row_step + height, col_step : col_step + breadth],
                    axis=(1, 2),
                )
            )
    return jnp.stack(pieces, axis=1).reshape(conv_grad.shape[0], 7, 7)


def xor_partner(value, axis, mask):
    return lax.ppermute(value, axis, [(i, i ^ mask) for i in range(lax.axis_size(axis))])


def butterfly_sum(parts, halving=(("col", 1), ("col", 2))):
    shapes = [p.shape for p in parts]
    flat = jnp.concatenate([p.reshape(-1) for p in parts])
    total = flat.shape[0]
    unit = 2 ** len(halving)
    flat = jnp.pad(flat, (0, -total % unit))
    doubling = []
    for axis in ("col", "row"):
        mask = 1
        while mask < lax.axis_size(axis):
            if (axis, mask) not in halving:
                doubling.append((axis, mask))
            mask *= 2
    sides = []
    for axis, mask in halving:
        half = flat.shape[0] // 2
        side = (lax.axis_index(axis) // mask) % 2
        keep = lax.dynamic_slice_in_dim(flat, side * half, half)
        send = lax.dynamic_slice_in_dim(flat, (1 - side) * half, half)
        flat = keep + xor_partner(send, axis, mask)
        sides.append(side)
    for axis, mask in doubling:
        flat = flat + xor_partner(flat, axis, mask)
    for (axis, mask), side in zip(reversed(halving), reversed(sides)):
        other = xor_partner(flat, axis, mask)
        flat = jnp.where(side == 0, jnp.concatenate([flat, other]), jnp.concatenate([other, flat]))
    out, start = [], 0
    for shape in shapes:
        size = math.prod(shape)
        out.append(flat[start : start + size].reshape(shape))
        start += size
    return tuple(out)


def product(form, left, right):
    return jnp.einsum(form, left, right, preferred_element_type=jnp.float32)


def mixing(conv_flat, image_flat, cotan_flat, ln_gain, ln_bias, w_in, b_in, w_out, layer_scale):
    average = jnp.mean(conv_flat, axis=0, keepdims=True)
    centred = conv_flat - average
    spread = jnp.mean(centred * centred, axis=0, keepdims=True)
    inverse = lax.rsqrt(spread + 1e-06)
    normed = centred * inverse
    ln_out = (normed * ln_gain[:, None] + ln_bias[:, None]).astype(jnp.bfloat16)
    pre_act = product("ch,cp->hp", w_in, ln_out) + b_in[:, None]
    act_out, gelu_pull = jax.vjp(jax.nn.gelu, pre_act)
    activ = act_out.astype(jnp.bfloat16)
    branch = product("hc,hp->cp", w_out, activ)
    scale_col = layer_scale[:, None]
    block_out = (image_flat.astype(jnp.float32) + scale_col * branch).astype(jnp.bfloat16)
    upstream = cotan_flat.astype(jnp.float32)
    scale_sum = jnp.sum(upstream * branch, axis=1)
    branch_grad = (scale_col * upstream).astype(jnp.bfloat16)
    w_out_sum = product("hp,cp->hc", activ, branch_grad)
    act_grad = product("hc,cp->hp", w_out, branch_grad)
    pre_grad = gelu_pull(act_grad)[0].astype(jnp.bfloat16)
    b_in_sum = jnp.sum(pre_grad.astype(jnp.float32), axis=1)
    w_in_sum = product("cp,hp->ch", ln_out, pre_grad)
    ln_grad = product("ch,hp->cp", w_in, pre_grad)
    gain_sum = jnp.sum(ln_grad * normed, axis=1)
    shift_sum = jnp.sum(ln_grad, axis=1)
    normed_grad = ln_grad * ln_gain[:, None]
    conv_grad = inverse * (
        normed_grad
        - jnp.mean(normed_grad, axis=0, keepdims=True)
        - normed * jnp.mean(normed_grad * normed, axis=0, keepdims=True)
    )
    return (block_out, conv_grad, (gain_sum, shift_sum, w_in_sum, b_in_sum, w_out_sum, scale_sum))


def local(image, cotangent, dw_kernel, dw_bias, ln_gain, ln_bias, w_in, b_in, w_out, layer_scale):
    channels, height, breadth = image.shape
    pixels = height * breadth
    padded = padded_2(image, (("row", 1), ("col", 2)), 3)
    conv_out = conv_seven(padded, dw_kernel) + dw_bias[:, None, None]
    block_flat, grad_flat, sums = mixing(
        conv_out.reshape(channels, pixels),
        image.reshape(channels, pixels),
        cotangent.reshape(channels, pixels),
        ln_gain,
        ln_bias,
        w_in,
        b_in,
        w_out,
        layer_scale,
    )
    gain_sum, shift_sum, w_in_sum, b_in_sum, w_out_sum, scale_sum = sums
    block_out = block_flat.reshape(channels, height, breadth)
    conv_grad = grad_flat.reshape(channels, height, breadth)
    flipped = dw_kernel[:, ::-1, ::-1]
    grad_col = padded_2(conv_grad, (("col", 2),), 3)
    grad_rows = padded_2(grad_col.astype(jnp.bfloat16), (("row", 1),), 3).astype(jnp.float32)
    grad_padded = jnp.concatenate(
        [grad_rows[:, :3, :], grad_col, grad_rows[:, height + 3 :, :]], axis=1
    )
    back = conv_seven(grad_padded, flipped)
    image_grad = (cotangent.astype(jnp.float32) + back).astype(jnp.bfloat16)
    kernel_sum = kernel_terms(conv_grad, padded)
    bias_sum = jnp.sum(conv_grad, axis=(1, 2))
    kernel_sum, bias_sum, gain_sum, shift_sum, w_in_sum, b_in_sum, w_out_sum, scale_sum = butterfly_sum(
        (kernel_sum, bias_sum, gain_sum, shift_sum, w_in_sum, b_in_sum, w_out_sum, scale_sum)
    )
    factor = 1.0 / math.sqrt(height * lax.axis_size("row") * breadth * lax.axis_size("col"))
    return (
        block_out,
        image_grad,
        factor * kernel_sum,
        factor * bias_sum,
        factor * gain_sum,
        factor * shift_sum,
        factor * w_in_sum,
        factor * b_in_sum,
        factor * w_out_sum,
        factor * scale_sum,
    )


def solution(mesh):
    in_specs = (
        P(None, "row", "col"),
        P(None, "row", "col"),
        P(),
        P(),
        P(),
        P(),
        P(),
        P(),
        P(),
        P(),
    )
    out_specs = (
        P(None, "row", "col"),
        P(None, "row", "col"),
        P(),
        P(),
        P(),
        P(),
        P(),
        P(),
        P(),
        P(),
    )
    return jax.shard_map(local, mesh=mesh, in_specs=in_specs, out_specs=out_specs, check_vma=False)
```

```python
import math

import jax
import jax.numpy as jnp
from jax import lax
from jax.sharding import PartitionSpec as P


def padded_2(block, sides, width):
    for axis, dim in sides:
        count = lax.axis_size(axis)
        forward = [(i, i + 1) for i in range(count - 1)]
        backward = [(target, source) for source, target in forward]
        low = lax.ppermute(
            lax.slice_in_dim(block, block.shape[dim] - width, None, axis=dim), axis, forward
        )
        high = lax.ppermute(lax.slice_in_dim(block, 0, width, axis=dim), axis, backward)
        block = jnp.concatenate([low, block, high], axis=dim)
    return block


def from_behind(value, axis, steps):
    count = lax.axis_size(axis)
    initial, last = (max(0, -steps), min(count, count - steps))
    return lax.ppermute(value, axis, [(source, source + steps) for source in range(initial, last)])


def conv_seven(padded, kernel):
    height = padded.shape[1] - 6
    breadth = padded.shape[2] - 6
    summed = jnp.zeros((padded.shape[0], height, breadth), jnp.float32)
    for row_step in range(7):
        for col_step in range(7):
            summed = (
                summed
                + kernel[:, row_step, col_step][:, None, None]
                * padded[:, row_step : row_step + height, col_step : col_step + breadth]
            )
    return summed


def kernel_terms(conv_grad, padded):
    height, breadth = (conv_grad.shape[1], conv_grad.shape[2])
    pieces = []
    for row_step in range(7):
        for col_step in range(7):
            pieces.append(
                jnp.sum(
                    conv_grad
                    * padded[:, row_step : row_step + height, col_step : col_step + breadth],
                    axis=(1, 2),
                )
            )
    return jnp.stack(pieces, axis=1).reshape(conv_grad.shape[0], 7, 7)


def xor_partner(value, axis, mask):
    return lax.ppermute(value, axis, [(i, i ^ mask) for i in range(lax.axis_size(axis))])


def butterfly_sum(parts, halving=(("col", 1), ("col", 2))):
    shapes = [p.shape for p in parts]
    flat = jnp.concatenate([p.reshape(-1) for p in parts])
    total = flat.shape[0]
    unit = 2 ** len(halving)
    flat = jnp.pad(flat, (0, -total % unit))
    doubling = []
    for axis in ("row", "col"):
        mask = 1
        while mask < lax.axis_size(axis):
            if (axis, mask) not in halving:
                doubling.append((axis, mask))
            mask *= 2
    sides = []
    for axis, mask in halving:
        half = flat.shape[0] // 2
        side = (lax.axis_index(axis) // mask) % 2
        keep = lax.dynamic_slice_in_dim(flat, side * half, half)
        send = lax.dynamic_slice_in_dim(flat, (1 - side) * half, half)
        flat = keep + xor_partner(send, axis, mask)
        sides.append(side)
    for axis, mask in doubling:
        flat = flat + xor_partner(flat, axis, mask)
    for (axis, mask), side in zip(reversed(halving), reversed(sides)):
        other = xor_partner(flat, axis, mask)
        flat = jnp.where(side == 0, jnp.concatenate([flat, other]), jnp.concatenate([other, flat]))
    out, start = [], 0
    for shape in shapes:
        size = math.prod(shape)
        out.append(flat[start : start + size].reshape(shape))
        start += size
    return tuple(out)


def product(form, left, right):
    return jnp.einsum(form, left, right, preferred_element_type=jnp.float32)


def mixing(conv_flat, image_flat, cotan_flat, ln_gain, ln_bias, w_in, b_in, w_out, layer_scale):
    average = jnp.mean(conv_flat, axis=0, keepdims=True)
    centred = conv_flat - average
    spread = jnp.mean(centred * centred, axis=0, keepdims=True)
    inverse = lax.rsqrt(spread + 1e-06)
    normed = centred * inverse
    ln_out = (normed * ln_gain[:, None] + ln_bias[:, None]).astype(jnp.bfloat16)
    pre_act = product("ch,cp->hp", w_in, ln_out) + b_in[:, None]
    act_out, gelu_pull = jax.vjp(jax.nn.gelu, pre_act)
    activ = act_out.astype(jnp.bfloat16)
    branch = product("hc,hp->cp", w_out, activ)
    scale_col = layer_scale[:, None]
    block_out = (image_flat.astype(jnp.float32) + scale_col * branch).astype(jnp.bfloat16)
    upstream = cotan_flat.astype(jnp.float32)
    scale_sum = jnp.sum(upstream * branch, axis=1)
    branch_grad = (scale_col * upstream).astype(jnp.bfloat16)
    w_out_sum = product("hp,cp->hc", activ, branch_grad)
    act_grad = product("hc,cp->hp", w_out, branch_grad)
    pre_grad = gelu_pull(act_grad)[0].astype(jnp.bfloat16)
    b_in_sum = jnp.sum(pre_grad.astype(jnp.float32), axis=1)
    w_in_sum = product("cp,hp->ch", ln_out, pre_grad)
    ln_grad = product("ch,hp->cp", w_in, pre_grad)
    gain_sum = jnp.sum(ln_grad * normed, axis=1)
    shift_sum = jnp.sum(ln_grad, axis=1)
    normed_grad = ln_grad * ln_gain[:, None]
    conv_grad = inverse * (
        normed_grad
        - jnp.mean(normed_grad, axis=0, keepdims=True)
        - normed * jnp.mean(normed_grad * normed, axis=0, keepdims=True)
    )
    return (block_out, conv_grad, (gain_sum, shift_sum, w_in_sum, b_in_sum, w_out_sum, scale_sum))


def local(image, cotangent, dw_kernel, dw_bias, ln_gain, ln_bias, w_in, b_in, w_out, layer_scale):
    channels, height, breadth = image.shape
    pixels = height * breadth
    padded = padded_2(image, (("col", 2), ("row", 1)), 3)
    conv_out = conv_seven(padded, dw_kernel) + dw_bias[:, None, None]
    block_flat, grad_flat, sums = mixing(
        conv_out.reshape(channels, pixels),
        image.reshape(channels, pixels),
        cotangent.reshape(channels, pixels),
        ln_gain,
        ln_bias,
        w_in,
        b_in,
        w_out,
        layer_scale,
    )
    gain_sum, shift_sum, w_in_sum, b_in_sum, w_out_sum, scale_sum = sums
    block_out = block_flat.reshape(channels, height, breadth)
    conv_grad = grad_flat.reshape(channels, height, breadth)
    flipped = dw_kernel[:, ::-1, ::-1]
    grad_col = padded_2(conv_grad, (("col", 2),), 3)
    grad_rows = padded_2(grad_col.astype(jnp.bfloat16), (("row", 1),), 3).astype(jnp.float32)
    grad_padded = jnp.concatenate(
        [grad_rows[:, :3, :], grad_col, grad_rows[:, height + 3 :, :]], axis=1
    )
    back = conv_seven(grad_padded, flipped)
    image_grad = (cotangent.astype(jnp.float32) + back).astype(jnp.bfloat16)
    kernel_sum = kernel_terms(conv_grad, padded)
    bias_sum = jnp.sum(conv_grad, axis=(1, 2))
    kernel_sum, bias_sum, gain_sum, shift_sum, w_in_sum, b_in_sum, w_out_sum, scale_sum = butterfly_sum(
        (kernel_sum, bias_sum, gain_sum, shift_sum, w_in_sum, b_in_sum, w_out_sum, scale_sum)
    )
    factor = 1.0 / math.sqrt(height * lax.axis_size("row") * breadth * lax.axis_size("col"))
    return (
        block_out,
        image_grad,
        factor * kernel_sum,
        factor * bias_sum,
        factor * gain_sum,
        factor * shift_sum,
        factor * w_in_sum,
        factor * b_in_sum,
        factor * w_out_sum,
        factor * scale_sum,
    )


def solution(mesh):
    in_specs = (
        P(None, "row", "col"),
        P(None, "row", "col"),
        P(),
        P(),
        P(),
        P(),
        P(),
        P(),
        P(),
        P(),
    )
    out_specs = (
        P(None, "row", "col"),
        P(None, "row", "col"),
        P(),
        P(),
        P(),
        P(),
        P(),
        P(),
        P(),
        P(),
    )
    return jax.shard_map(local, mesh=mesh, in_specs=in_specs, out_specs=out_specs, check_vma=False)
```

```python
import math

import jax
import jax.numpy as jnp
from jax import lax
from jax.sharding import PartitionSpec as P


def padded_2(block, sides, width):
    for axis, dim in sides:
        count = lax.axis_size(axis)
        forward = [(i, i + 1) for i in range(count - 1)]
        backward = [(target, source) for source, target in forward]
        low = lax.ppermute(
            lax.slice_in_dim(block, block.shape[dim] - width, None, axis=dim), axis, forward
        )
        high = lax.ppermute(lax.slice_in_dim(block, 0, width, axis=dim), axis, backward)
        block = jnp.concatenate([low, block, high], axis=dim)
    return block


def from_behind(value, axis, steps):
    count = lax.axis_size(axis)
    initial, last = (max(0, -steps), min(count, count - steps))
    return lax.ppermute(value, axis, [(source, source + steps) for source in range(initial, last)])


def conv_seven(padded, kernel):
    height = padded.shape[1] - 6
    breadth = padded.shape[2] - 6
    summed = jnp.zeros((padded.shape[0], height, breadth), jnp.float32)
    for row_step in range(7):
        for col_step in range(7):
            summed = (
                summed
                + kernel[:, row_step, col_step][:, None, None]
                * padded[:, row_step : row_step + height, col_step : col_step + breadth]
            )
    return summed


def kernel_terms(conv_grad, padded):
    height, breadth = (conv_grad.shape[1], conv_grad.shape[2])
    pieces = []
    for row_step in range(7):
        for col_step in range(7):
            pieces.append(
                jnp.sum(
                    conv_grad
                    * padded[:, row_step : row_step + height, col_step : col_step + breadth],
                    axis=(1, 2),
                )
            )
    return jnp.stack(pieces, axis=1).reshape(conv_grad.shape[0], 7, 7)


def xor_partner(value, axis, mask):
    return lax.ppermute(value, axis, [(i, i ^ mask) for i in range(lax.axis_size(axis))])


def butterfly_sum(parts, halving=(("col", 1), ("col", 2))):
    shapes = [p.shape for p in parts]
    flat = jnp.concatenate([p.reshape(-1) for p in parts])
    total = flat.shape[0]
    unit = 2 ** len(halving)
    flat = jnp.pad(flat, (0, -total % unit))
    doubling = []
    for axis in ("row", "col"):
        mask = 1
        while mask < lax.axis_size(axis):
            if (axis, mask) not in halving:
                doubling.append((axis, mask))
            mask *= 2
    sides = []
    for axis, mask in halving:
        half = flat.shape[0] // 2
        side = (lax.axis_index(axis) // mask) % 2
        keep = lax.dynamic_slice_in_dim(flat, side * half, half)
        send = lax.dynamic_slice_in_dim(flat, (1 - side) * half, half)
        flat = keep + xor_partner(send, axis, mask)
        sides.append(side)
    for axis, mask in doubling:
        flat = flat + xor_partner(flat, axis, mask)
    for (axis, mask), side in zip(reversed(halving), reversed(sides)):
        other = xor_partner(flat, axis, mask)
        flat = lax.dynamic_update_slice_in_dim(jnp.concatenate([other, other]), flat, side * flat.shape[0], 0)
    out, start = [], 0
    for shape in shapes:
        size = math.prod(shape)
        out.append(flat[start : start + size].reshape(shape))
        start += size
    return tuple(out)


def product(form, left, right):
    return jnp.einsum(form, left, right, preferred_element_type=jnp.float32)


def mixing(conv_flat, image_flat, cotan_flat, ln_gain, ln_bias, w_in, b_in, w_out, layer_scale):
    average = jnp.mean(conv_flat, axis=0, keepdims=True)
    centred = conv_flat - average
    spread = jnp.mean(centred * centred, axis=0, keepdims=True)
    inverse = lax.rsqrt(spread + 1e-06)
    normed = centred * inverse
    ln_out = (normed * ln_gain[:, None] + ln_bias[:, None]).astype(jnp.bfloat16)
    pre_act = product("ch,cp->hp", w_in, ln_out) + b_in[:, None]
    act_out, gelu_pull = jax.vjp(jax.nn.gelu, pre_act)
    activ = act_out.astype(jnp.bfloat16)
    branch = product("hc,hp->cp", w_out, activ)
    scale_col = layer_scale[:, None]
    block_out = (image_flat.astype(jnp.float32) + scale_col * branch).astype(jnp.bfloat16)
    upstream = cotan_flat.astype(jnp.float32)
    scale_sum = jnp.sum(upstream * branch, axis=1)
    branch_grad = (scale_col * upstream).astype(jnp.bfloat16)
    w_out_sum = product("hp,cp->hc", activ, branch_grad)
    act_grad = product("hc,cp->hp", w_out, branch_grad)
    pre_grad = gelu_pull(act_grad)[0].astype(jnp.bfloat16)
    b_in_sum = jnp.sum(pre_grad.astype(jnp.float32), axis=1)
    w_in_sum = product("cp,hp->ch", ln_out, pre_grad)
    ln_grad = product("ch,hp->cp", w_in, pre_grad)
    gain_sum = jnp.sum(ln_grad * normed, axis=1)
    shift_sum = jnp.sum(ln_grad, axis=1)
    normed_grad = ln_grad * ln_gain[:, None]
    conv_grad = inverse * (
        normed_grad
        - jnp.mean(normed_grad, axis=0, keepdims=True)
        - normed * jnp.mean(normed_grad * normed, axis=0, keepdims=True)
    )
    return (block_out, conv_grad, (gain_sum, shift_sum, w_in_sum, b_in_sum, w_out_sum, scale_sum))


def local(image, cotangent, dw_kernel, dw_bias, ln_gain, ln_bias, w_in, b_in, w_out, layer_scale):
    channels, height, breadth = image.shape
    pixels = height * breadth
    padded = padded_2(image, (("col", 2), ("row", 1)), 3)
    conv_out = conv_seven(padded, dw_kernel) + dw_bias[:, None, None]
    block_flat, grad_flat, sums = mixing(
        conv_out.reshape(channels, pixels),
        image.reshape(channels, pixels),
        cotangent.reshape(channels, pixels),
        ln_gain,
        ln_bias,
        w_in,
        b_in,
        w_out,
        layer_scale,
    )
    gain_sum, shift_sum, w_in_sum, b_in_sum, w_out_sum, scale_sum = sums
    block_out = block_flat.reshape(channels, height, breadth)
    conv_grad = grad_flat.reshape(channels, height, breadth)
    flipped = dw_kernel[:, ::-1, ::-1]
    grad_col = padded_2(conv_grad, (("col", 2),), 3)
    grad_rows = padded_2(grad_col.astype(jnp.bfloat16), (("row", 1),), 3).astype(jnp.float32)
    grad_padded = jnp.concatenate(
        [grad_rows[:, :3, :], grad_col, grad_rows[:, height + 3 :, :]], axis=1
    )
    back = conv_seven(grad_padded, flipped)
    image_grad = (cotangent.astype(jnp.float32) + back).astype(jnp.bfloat16)
    kernel_sum = kernel_terms(conv_grad, padded)
    bias_sum = jnp.sum(conv_grad, axis=(1, 2))
    kernel_sum, bias_sum, gain_sum, shift_sum, w_in_sum, b_in_sum, w_out_sum, scale_sum = butterfly_sum(
        (kernel_sum, bias_sum, gain_sum, shift_sum, w_in_sum, b_in_sum, w_out_sum, scale_sum)
    )
    factor = 1.0 / math.sqrt(height * lax.axis_size("row") * breadth * lax.axis_size("col"))
    return (
        block_out,
        image_grad,
        factor * kernel_sum,
        factor * bias_sum,
        factor * gain_sum,
        factor * shift_sum,
        factor * w_in_sum,
        factor * b_in_sum,
        factor * w_out_sum,
        factor * scale_sum,
    )


def solution(mesh):
    in_specs = (
        P(None, "row", "col"),
        P(None, "row", "col"),
        P(),
        P(),
        P(),
        P(),
        P(),
        P(),
        P(),
        P(),
    )
    out_specs = (
        P(None, "row", "col"),
        P(None, "row", "col"),
        P(),
        P(),
        P(),
        P(),
        P(),
        P(),
        P(),
        P(),
    )
    return jax.shard_map(local, mesh=mesh, in_specs=in_specs, out_specs=out_specs, check_vma=False)
```

```python
import math

import jax
import jax.numpy as jnp
from jax import lax
from jax.sharding import PartitionSpec as P


def padded_2(block, sides, width):
    for axis, dim in sides:
        count = lax.axis_size(axis)
        forward = [(i, i + 1) for i in range(count - 1)]
        backward = [(target, source) for source, target in forward]
        low = lax.ppermute(
            lax.slice_in_dim(block, block.shape[dim] - width, None, axis=dim), axis, forward
        )
        high = lax.ppermute(lax.slice_in_dim(block, 0, width, axis=dim), axis, backward)
        block = jnp.concatenate([low, block, high], axis=dim)
    return block


def from_behind(value, axis, steps):
    count = lax.axis_size(axis)
    initial, last = (max(0, -steps), min(count, count - steps))
    return lax.ppermute(value, axis, [(source, source + steps) for source in range(initial, last)])


def conv_seven(padded, kernel):
    height = padded.shape[1] - 6
    breadth = padded.shape[2] - 6
    summed = jnp.zeros((padded.shape[0], height, breadth), jnp.float32)
    for row_step in range(7):
        for col_step in range(7):
            summed = (
                summed
                + kernel[:, row_step, col_step][:, None, None]
                * padded[:, row_step : row_step + height, col_step : col_step + breadth]
            )
    return summed


def kernel_terms(conv_grad, padded):
    height, breadth = (conv_grad.shape[1], conv_grad.shape[2])
    pieces = []
    for row_step in range(7):
        for col_step in range(7):
            pieces.append(
                jnp.sum(
                    conv_grad
                    * padded[:, row_step : row_step + height, col_step : col_step + breadth],
                    axis=(1, 2),
                )
            )
    return jnp.stack(pieces, axis=1).reshape(conv_grad.shape[0], 7, 7)


def xor_partner(value, axis, mask):
    return lax.ppermute(value, axis, [(i, i ^ mask) for i in range(lax.axis_size(axis))])


def butterfly_sum(parts, halving=(("col", 1), ("col", 16))):
    shapes = [p.shape for p in parts]
    flat = jnp.concatenate([p.reshape(-1) for p in parts])
    total = flat.shape[0]
    unit = 2 ** len(halving)
    flat = jnp.pad(flat, (0, -total % unit))
    doubling = []
    for axis in ("row", "col"):
        mask = 1
        while mask < lax.axis_size(axis):
            if (axis, mask) not in halving:
                doubling.append((axis, mask))
            mask *= 2
    sides = []
    for axis, mask in halving:
        half = flat.shape[0] // 2
        side = (lax.axis_index(axis) // mask) % 2
        keep = lax.dynamic_slice_in_dim(flat, side * half, half)
        send = lax.dynamic_slice_in_dim(flat, (1 - side) * half, half)
        flat = keep + xor_partner(send, axis, mask)
        sides.append(side)
    for axis, mask in doubling:
        flat = flat + xor_partner(flat, axis, mask)
    for (axis, mask), side in zip(reversed(halving), reversed(sides)):
        other = xor_partner(flat, axis, mask)
        flat = jnp.where(side == 0, jnp.concatenate([flat, other]), jnp.concatenate([other, flat]))
    out, start = [], 0
    for shape in shapes:
        size = math.prod(shape)
        out.append(flat[start : start + size].reshape(shape))
        start += size
    return tuple(out)


def product(form, left, right):
    return jnp.einsum(form, left, right, preferred_element_type=jnp.float32)


def mixing(conv_flat, image_flat, cotan_flat, ln_gain, ln_bias, w_in, b_in, w_out, layer_scale):
    average = jnp.mean(conv_flat, axis=0, keepdims=True)
    centred = conv_flat - average
    spread = jnp.mean(centred * centred, axis=0, keepdims=True)
    inverse = lax.rsqrt(spread + 1e-06)
    normed = centred * inverse
    ln_out = (normed * ln_gain[:, None] + ln_bias[:, None]).astype(jnp.bfloat16)
    pre_act = product("ch,cp->hp", w_in, ln_out) + b_in[:, None]
    act_out, gelu_pull = jax.vjp(jax.nn.gelu, pre_act)
    activ = act_out.astype(jnp.bfloat16)
    branch = product("hc,hp->cp", w_out, activ)
    scale_col = layer_scale[:, None]
    block_out = (image_flat.astype(jnp.float32) + scale_col * branch).astype(jnp.bfloat16)
    upstream = cotan_flat.astype(jnp.float32)
    scale_sum = jnp.sum(upstream * branch, axis=1)
    branch_grad = (scale_col * upstream).astype(jnp.bfloat16)
    w_out_sum = product("hp,cp->hc", activ, branch_grad)
    act_grad = product("hc,cp->hp", w_out, branch_grad)
    pre_grad = gelu_pull(act_grad)[0].astype(jnp.bfloat16)
    b_in_sum = jnp.sum(pre_grad.astype(jnp.float32), axis=1)
    w_in_sum = product("cp,hp->ch", ln_out, pre_grad)
    ln_grad = product("ch,hp->cp", w_in, pre_grad)
    gain_sum = jnp.sum(ln_grad * normed, axis=1)
    shift_sum = jnp.sum(ln_grad, axis=1)
    normed_grad = ln_grad * ln_gain[:, None]
    conv_grad = inverse * (
        normed_grad
        - jnp.mean(normed_grad, axis=0, keepdims=True)
        - normed * jnp.mean(normed_grad * normed, axis=0, keepdims=True)
    )
    return (block_out, conv_grad, (gain_sum, shift_sum, w_in_sum, b_in_sum, w_out_sum, scale_sum))


def local(image, cotangent, dw_kernel, dw_bias, ln_gain, ln_bias, w_in, b_in, w_out, layer_scale):
    channels, height, breadth = image.shape
    pixels = height * breadth
    padded = padded_2(image, (("col", 2), ("row", 1)), 3)
    conv_out = conv_seven(padded, dw_kernel) + dw_bias[:, None, None]
    block_flat, grad_flat, sums = mixing(
        conv_out.reshape(channels, pixels),
        image.reshape(channels, pixels),
        cotangent.reshape(channels, pixels),
        ln_gain,
        ln_bias,
        w_in,
        b_in,
        w_out,
        layer_scale,
    )
    gain_sum, shift_sum, w_in_sum, b_in_sum, w_out_sum, scale_sum = sums
    block_out = block_flat.reshape(channels, height, breadth)
    conv_grad = grad_flat.reshape(channels, height, breadth)
    flipped = dw_kernel[:, ::-1, ::-1]
    grad_col = padded_2(conv_grad, (("col", 2),), 3)
    grad_rows = padded_2(grad_col.astype(jnp.bfloat16), (("row", 1),), 3).astype(jnp.float32)
    grad_padded = jnp.concatenate(
        [grad_rows[:, :3, :], grad_col, grad_rows[:, height + 3 :, :]], axis=1
    )
    back = conv_seven(grad_padded, flipped)
    image_grad = (cotangent.astype(jnp.float32) + back).astype(jnp.bfloat16)
    kernel_sum = kernel_terms(conv_grad, padded)
    bias_sum = jnp.sum(conv_grad, axis=(1, 2))
    kernel_sum, bias_sum, gain_sum, shift_sum, w_in_sum, b_in_sum, w_out_sum, scale_sum = butterfly_sum(
        (kernel_sum, bias_sum, gain_sum, shift_sum, w_in_sum, b_in_sum, w_out_sum, scale_sum)
    )
    factor = 1.0 / math.sqrt(height * lax.axis_size("row") * breadth * lax.axis_size("col"))
    return (
        block_out,
        image_grad,
        factor * kernel_sum,
        factor * bias_sum,
        factor * gain_sum,
        factor * shift_sum,
        factor * w_in_sum,
        factor * b_in_sum,
        factor * w_out_sum,
        factor * scale_sum,
    )


def solution(mesh):
    in_specs = (
        P(None, "row", "col"),
        P(None, "row", "col"),
        P(),
        P(),
        P(),
        P(),
        P(),
        P(),
        P(),
        P(),
    )
    out_specs = (
        P(None, "row", "col"),
        P(None, "row", "col"),
        P(),
        P(),
        P(),
        P(),
        P(),
        P(),
        P(),
        P(),
    )
    return jax.shard_map(local, mesh=mesh, in_specs=in_specs, out_specs=out_specs, check_vma=False)
```
